256 devices in a mesh: seq: 4 (over y), ch: 64 (over x, z, core).
Axes of the slice: x: 4, y: 4, z: 8, core: 2. Of those that a mesh axis runs over, the one named last changes fastest.
Arguments:
- tokens: bfloat16 [1024, 8192], P('seq', 'ch'), may hold values from -6 to 6
- in_weight: bfloat16 [8192, 3, 8192], P(None, None, 'ch'), may hold values from -0.0625 to 0.0625
- short_taps: float32 [3, 3, 8192], P(None, None, 'ch'), may hold values from -3 to 3
- decay_rates: float32 [16, 512], P(None, 'ch'), may hold values from 0.05 to 200
- residues: float32 [16, 512], P(None, 'ch'), may hold values from -0.18 to 0.18
- out_weight: bfloat16 [8192, 8192], P('ch'), may hold values from -0.1875 to 0.1875
Outputs:
- mixed: bfloat16 [1024, 8192], P('seq', 'ch')
The draws below stay inside these ranges and needn't reach their ends.
All inputs are finite; a program needn't handle non-finite values.
Results may differ from the reference program's by a relative error of at most 0.007.
Values may be sent and summed in bfloat16 or wider, within the bound.
No kernel may reach another device: no remote copies, remote signals or barrier semaphores. Data moves between devices by JAX's collectives and lax.ppermute only.
A program may use at most 64 MiB of HBM per device.

```python
import math
import jax
import jax.numpy as jnp
from jax import lax

D = 8192
MODES = 16
GROUP = 16
TAPS = 3
TOKENS = 1024
FILTERS = 512


def with_spikes(values, own_key, source, target, blocks, factor):
    owner, partner = [(jnp.arange(values.shape[dim]) // (values.shape[dim] // blocks)).reshape([-1 if axis == dim else 1 for axis in range(values.ndim)]) for dim in (source, target)]
    chosen = jax.random.permutation(own_key, blocks)[partner]
    strong = (owner == chosen) | (owner == (partner + blocks // 2) % blocks)
    return jnp.where(strong, factor * values, values)


def block_scale(own_key, shape, shards, low, high):
    def one(axis_at, blocks):
        draws = jax.random.uniform(jax.random.fold_in(jax.random.fold_in(own_key, 6), axis_at), (blocks,), jnp.float32, low / len(shards), high / len(shards))
        return jnp.repeat(jnp.exp(draws), shape[axis_at] // blocks).reshape((-1,) + (1,) * (len(shape) - axis_at - 1))

    level = one(*shards[0])
    for cut in shards[1:]:
        level = level * one(*cut)
    return level


def gaussian(key, extent, width, bound, pieces=(), kind=jnp.bfloat16):
    values = width * jax.random.normal(key, extent, jnp.float32)
    if pieces:
        values = values * block_scale(key, extent, pieces, -0.22, 0.18)
    return jnp.clip(values, -bound, bound).astype(kind)


def heavy_noise(rng, shape, spread, reach, shards, heavy, kind=jnp.bfloat16):
    values = spread * jax.random.normal(rng, shape, jnp.float32)
    if shards:
        values = values * block_scale(rng, shape, shards, -0.22, 0.18)
    return jnp.clip(with_spikes(values, jax.random.fold_in(rng, 3), *heavy), -reach, reach).astype(kind)


def setup_inputs(seed: int = 0) -> dict:
    streams_of = jax.random.split(jax.random.key(seed), 7)
    tokens = gaussian(streams_of[0], (TOKENS, D), 1.0, 6.0, ((0, 4), (1, 64)))
    in_weight = gaussian(streams_of[1], (D, 3, D), D ** -0.5, 0.0625, ((2, 64),))
    short_taps = gaussian(streams_of[2], (TAPS, 3, D), 0.6, 3.0, ((2, 64),), jnp.float32)
    decay_rates = jnp.clip(jnp.exp(math.log(200.0) - 8.2940496 * jax.random.uniform(streams_of[3], (MODES, FILTERS), jnp.float32) ** block_scale(streams_of[3], (MODES, FILTERS), ((1, 64),), -0.2, 0.2)), 0.05, 200.0)
    residues = gaussian(streams_of[4], (MODES, FILTERS), 0.03, 0.18, ((1, 64),), jnp.float32)
    out_weight = heavy_noise(streams_of[5], (D, D), D ** -0.5, 0.1875, ((0, 64),), (0, 1, 64, 4.0))
    return dict(tokens=tokens, in_weight=in_weight, short_taps=short_taps, decay_rates=decay_rates, residues=residues, out_weight=out_weight)


def reference(tokens, in_weight, short_taps, decay_rates, residues, out_weight):
    projected = jnp.dot(tokens, in_weight.reshape(D, 3 * D), preferred_element_type=jnp.float32).astype(jnp.bfloat16)
    padded = jnp.concatenate([jnp.zeros((TAPS - 1, 3 * D), jnp.float32), projected.astype(jnp.float32)], axis=0)
    flat_taps = short_taps.reshape(TAPS, 3 * D)
    filtered = jnp.zeros((TOKENS, 3 * D), jnp.float32)
    for shift_back in range(TAPS):
        filtered = filtered + flat_taps[shift_back] * padded[TAPS - 1 - shift_back:TAPS - 1 - shift_back + TOKENS]
    query_stream = filtered[:, :D]
    gated_in = filtered[:, D:2 * D] * filtered[:, 2 * D:]
    per_step = jnp.repeat(jnp.exp(-decay_rates / TOKENS), GROUP, axis=1)
    weights = jnp.repeat(residues, GROUP, axis=1)

    def advance(state, row):
        state = per_step * state + row[None, :]
        return state, jnp.sum(weights * state, axis=0)

    start_state = jnp.zeros((MODES, D), jnp.float32)
    final_state, convolved = lax.scan(advance, start_state, gated_in)
    gated_out = (query_stream * convolved).astype(jnp.bfloat16)
    return jnp.dot(gated_out, out_weight, preferred_element_type=jnp.float32).astype(jnp.bfloat16)
```

```python
import math

import jax
import jax.numpy as jnp
from jax import lax
from jax.sharding import PartitionSpec as P

TAPS = 3


def passed_along(block, axis, distance):
    devices = range(lax.axis_size(axis))
    route = [(i - distance, i) for i in devices if i - distance in devices]
    return lax.ppermute(block, axis, route)


def on_device(tokens, in_weight, short_taps, decay_rates, residues, out_weight):
    rows_here = tokens.shape[0]
    width_here = in_weight.shape[2]
    model_width = in_weight.shape[0]
    filter_count = decay_rates.shape[1]
    mode_count = decay_rates.shape[0]
    group_width = width_here // filter_count
    tokens_all = rows_here * lax.axis_size("seq")
    flat_weight = in_weight.reshape(model_width, 3 * width_here)
    gathered = lax.all_gather(tokens, "ch", axis=1, tiled=True)
    projected = jnp.dot(gathered, flat_weight, preferred_element_type=jnp.float32).astype(
        jnp.bfloat16
    )
    previous = passed_along(projected[rows_here - (TAPS - 1) :], "seq", 1)
    padded = jnp.concatenate([previous, projected], axis=0).astype(jnp.float32)
    flat_taps = short_taps.reshape(TAPS, 3 * width_here)
    filtered = jnp.zeros((rows_here, 3 * width_here), jnp.float32)
    for shift_back in range(TAPS):
        filtered = (
            filtered
            + flat_taps[shift_back]
            * padded[TAPS - 1 - shift_back : TAPS - 1 - shift_back + rows_here]
        )
    query_stream = filtered[:, :width_here]
    gated_in = filtered[:, width_here : 2 * width_here] * filtered[:, 2 * width_here :]
    block_len = math.gcd(rows_here, 128)
    block_count = rows_here // block_len
    scaled_rates = decay_rates / tokens_all
    offsets_in = jnp.arange(block_len, dtype=jnp.float32)
    distance = jnp.arange(block_len)[:, None] - jnp.arange(block_len)[None, :]
    lag = jnp.maximum(distance, 0).astype(jnp.float32)
    toeplitz = jnp.where(
        (distance >= 0)[None],
        jnp.sum(residues[:, :, None, None] * jnp.exp(-scaled_rates[:, :, None, None] * lag), axis=0),
        0.0,
    )
    blocks_in = gated_in.reshape(block_count, block_len, filter_count, group_width)
    local_part = jnp.einsum("gts,bsgi->btgi", toeplitz, blocks_in, precision=lax.Precision.HIGHEST)
    end_weights = jnp.exp(-scaled_rates[:, :, None] * (block_len - 1 - offsets_in)[None, None, :])
    block_ends = jnp.einsum(
        "mgs,bsgi->bmgi", end_weights, blocks_in, precision=lax.Precision.HIGHEST
    )
    inner_decay = jnp.exp(-scaled_rates * block_len)[:, :, None]
    running = jnp.zeros((mode_count, filter_count, group_width), jnp.float32)
    starts_list = []
    for block_number in range(block_count):
        starts_list.append(running)
        running = inner_decay * running + block_ends[block_number]
    local_starts = jnp.stack(starts_list, axis=0)
    end_state = running.reshape(mode_count, width_here)
    incoming = jnp.zeros((mode_count, width_here), jnp.float32)
    for hops in range(1, lax.axis_size("seq")):
        decayed = jnp.repeat(jnp.exp(-scaled_rates * (rows_here * (hops - 1))), group_width, axis=1)
        incoming = incoming + decayed * passed_along(end_state, "seq", hops)
    block_offsets = (jnp.arange(block_count, dtype=jnp.float32) * block_len)[:, None, None]
    start_decay = jnp.exp(-scaled_rates[None] * block_offsets)
    block_starts = (
        local_starts
        + start_decay[..., None] * incoming.reshape(mode_count, filter_count, group_width)[None]
    )
    carry_weights = residues[None] * jnp.exp(
        -scaled_rates[None] * (offsets_in + 1.0)[:, None, None]
    )
    carried = jnp.einsum(
        "tmg,bmgi->btgi", carry_weights, block_starts, precision=lax.Precision.HIGHEST
    )
    convolved = (local_part + carried).reshape(rows_here, width_here)
    gated_out = (query_stream * convolved).astype(jnp.bfloat16)
    turned = lax.psum_scatter(
        lax.dot_general(
            out_weight, gated_out, (((0,), (1,)), ((), ())), preferred_element_type=jnp.float32
        ),
        "ch",
        scatter_dimension=0,
        tiled=True,
    )
    mixed = turned.T.astype(jnp.bfloat16)
    return mixed


def solution(mesh):
    in_specs = (
        P("seq", "ch"),
        P(None, None, "ch"),
        P(None, None, "ch"),
        P(None, "ch"),
        P(None, "ch"),
        P("ch", None),
    )
    out_specs = P("seq", "ch")
    return jax.shard_map(
        on_device, mesh=mesh, in_specs=in_specs, out_specs=out_specs, check_vma=False
    )
```

```python
import math

import jax
import jax.numpy as jnp
from jax import lax
from jax.sharding import Mesh, PartitionSpec as P

TAPS = 3


def passed_along(block, axis, distance):
    devices = range(lax.axis_size(axis))
    route = [(i - distance, i) for i in devices if i - distance in devices]
    return lax.ppermute(block, axis, route)


CH = ("x", "z", "core")


def gather_features(tokens):
    rows, width = tokens.shape
    chips = lax.axis_size(("x", "z"))
    spread = jnp.broadcast_to(tokens[None], (chips,) + tokens.shape)
    same_core = lax.all_to_all(spread, ("x", "z"), 0, 0, tiled=True)
    both = jnp.broadcast_to(same_core[None], (2,) + same_core.shape)
    every = lax.all_to_all(both, "core", 0, 0, tiled=True)
    return every.transpose(2, 1, 0, 3).reshape(rows, 2 * chips * width)


def summed_over(parts, axis):
    got = lax.all_to_all(parts.astype(jnp.bfloat16), axis, 0, 0, tiled=True)
    return jnp.sum(got.astype(jnp.float32), axis=0)


def sum_over_channels(partial):
    nx, nz = lax.axis_size("x"), lax.axis_size("z")
    width = partial.shape[0] // (nx * nz * 2)
    arranged = partial.reshape(nx, nz, 2, width, partial.shape[1]).transpose(2, 0, 1, 3, 4)
    by_core = summed_over(arranged, "core")
    by_x = summed_over(by_core, "x")
    return summed_over(by_x, "z")


def on_device(tokens, in_weight, short_taps, decay_rates, residues, out_weight):
    rows_here = tokens.shape[0]
    width_here = in_weight.shape[2]
    model_width = in_weight.shape[0]
    filter_count = decay_rates.shape[1]
    mode_count = decay_rates.shape[0]
    group_width = width_here // filter_count
    tokens_all = rows_here * lax.axis_size("seq")
    flat_weight = in_weight.reshape(model_width, 3 * width_here)
    gathered = gather_features(tokens)
    projected = jnp.dot(gathered, flat_weight, preferred_element_type=jnp.float32).astype(
        jnp.bfloat16
    )
    previous = passed_along(projected[rows_here - (TAPS - 1) :], "seq", 1)
    padded = jnp.concatenate([previous, projected], axis=0).astype(jnp.float32)
    flat_taps = short_taps.reshape(TAPS, 3 * width_here)
    filtered = jnp.zeros((rows_here, 3 * width_here), jnp.float32)
    for shift_back in range(TAPS):
        filtered = (
            filtered
            + flat_taps[shift_back]
            * padded[TAPS - 1 - shift_back : TAPS - 1 - shift_back + rows_here]
        )
    query_stream = filtered[:, :width_here]
    gated_in = filtered[:, width_here : 2 * width_here] * filtered[:, 2 * width_here :]
    block_len = math.gcd(rows_here, 128)
    block_count = rows_here // block_len
    scaled_rates = decay_rates / tokens_all
    offsets_in = jnp.arange(block_len, dtype=jnp.float32)
    distance = jnp.arange(block_len)[:, None] - jnp.arange(block_len)[None, :]
    lag = jnp.maximum(distance, 0).astype(jnp.float32)
    toeplitz = jnp.where(
        (distance >= 0)[None],
        jnp.sum(residues[:, :, None, None] * jnp.exp(-scaled_rates[:, :, None, None] * lag), axis=0),
        0.0,
    )
    blocks_in = gated_in.reshape(block_count, block_len, filter_count, group_width)
    local_part = jnp.einsum("gts,bsgi->btgi", toeplitz, blocks_in, precision=lax.Precision.HIGHEST)
    end_weights = jnp.exp(-scaled_rates[:, :, None] * (block_len - 1 - offsets_in)[None, None, :])
    block_ends = jnp.einsum(
        "mgs,bsgi->bmgi", end_weights, blocks_in, precision=lax.Precision.HIGHEST
    )
    inner_decay = jnp.exp(-scaled_rates * block_len)[:, :, None]
    running = jnp.zeros((mode_count, filter_count, group_width), jnp.float32)
    starts_list = []
    for block_number in range(block_count):
        starts_list.append(running)
        running = inner_decay * running + block_ends[block_number]
    local_starts = jnp.stack(starts_list, axis=0)
    end_state = running.reshape(mode_count, width_here)
    incoming = jnp.zeros((mode_count, width_here), jnp.float32)
    for hops in range(1, lax.axis_size("seq")):
        decayed = jnp.repeat(jnp.exp(-scaled_rates * (rows_here * (hops - 1))), group_width, axis=1)
        incoming = incoming + decayed * passed_along(end_state, "seq", hops)
    block_offsets = (jnp.arange(block_count, dtype=jnp.float32) * block_len)[:, None, None]
    start_decay = jnp.exp(-scaled_rates[None] * block_offsets)
    block_starts = (
        local_starts
        + start_decay[..., None] * incoming.reshape(mode_count, filter_count, group_width)[None]
    )
    carry_weights = residues[None] * jnp.exp(
        -scaled_rates[None] * (offsets_in + 1.0)[:, None, None]
    )
    carried = jnp.einsum(
        "tmg,bmgi->btgi", carry_weights, block_starts, precision=lax.Precision.HIGHEST
    )
    convolved = (local_part + carried).reshape(rows_here, width_here)
    gated_out = (query_stream * convolved).astype(jnp.bfloat16)
    turned = sum_over_channels(
        lax.dot_general(
            out_weight, gated_out, (((0,), (1,)), ((), ())), preferred_element_type=jnp.float32
        )
    )
    mixed = turned.T.astype(jnp.bfloat16)
    return mixed


def fine_mesh(mesh):
    devices = mesh.devices
    coords = [d.coords for d in devices.flat]
    nx = len({c[0] for c in coords})
    nz = len({c[2] for c in coords})
    return Mesh(devices.reshape(devices.shape[0], nx, nz, devices.shape[1] // (nx * nz)), ("seq",) + CH)


def solution(mesh):
    in_specs = (
        P("seq", CH),
        P(None, None, CH),
        P(None, None, CH),
        P(None, CH),
        P(None, CH),
        P(CH, None),
    )
    out_specs = P("seq", CH)
    return jax.shard_map(
        on_device, mesh=fine_mesh(mesh), in_specs=in_specs, out_specs=out_specs, check_vma=False
    )
```

```python
import math

import jax
import jax.numpy as jnp
from jax import lax
from jax.sharding import Mesh, PartitionSpec as P

TAPS = 3


def passed_along(block, axis, distance):
    devices = range(lax.axis_size(axis))
    route = [(i - distance, i) for i in devices if i - distance in devices]
    return lax.ppermute(block, axis, route)


CH = ("x", "z", "core")


def gather_features(tokens):
    rows, width = tokens.shape
    chips = lax.axis_size(("x", "z"))
    spread = jnp.broadcast_to(tokens[None], (chips,) + tokens.shape)
    same_core = lax.all_to_all(spread, ("x", "z"), 0, 0, tiled=True)
    both = jnp.broadcast_to(same_core[None], (2,) + same_core.shape)
    every = lax.all_to_all(both, "core", 0, 0, tiled=True)
    return every.transpose(2, 1, 0, 3).reshape(rows, 2 * chips * width)


def summed_over(parts, axis):
    got = lax.all_to_all(parts.astype(jnp.bfloat16), axis, 0, 0, tiled=True)
    return jnp.sum(got.astype(jnp.float32), axis=0)


def pair_rows(out_weight):
    rows, model_width = out_weight.shape
    nx, nz = lax.axis_size("x"), lax.axis_size("z")
    width = model_width // (nx * nz * 2)
    split = out_weight.reshape(rows, nx, nz, 2, width).transpose(3, 0, 1, 2, 4)
    return lax.all_to_all(split, "core", 0, 0, tiled=True)


def project_out(weight_pair, gated_out):
    both = jnp.broadcast_to(gated_out[None], (2,) + gated_out.shape)
    inputs_pair = lax.all_to_all(both, "core", 0, 0, tiled=True)
    return jnp.einsum(
        "crxzw,ctr->xzwt", weight_pair, inputs_pair, preferred_element_type=jnp.float32
    )


def sum_over_channels(partial):
    by_x = summed_over(partial, "x")
    return summed_over(by_x, "z")


def on_device(tokens, in_weight, short_taps, decay_rates, residues, out_weight):
    rows_here = tokens.shape[0]
    width_here = in_weight.shape[2]
    model_width = in_weight.shape[0]
    filter_count = decay_rates.shape[1]
    mode_count = decay_rates.shape[0]
    group_width = width_here // filter_count
    tokens_all = rows_here * lax.axis_size("seq")
    flat_weight = in_weight.reshape(model_width, 3 * width_here)
    out_weight_pair = pair_rows(out_weight)
    gathered = gather_features(tokens)
    projected = jnp.dot(gathered, flat_weight, preferred_element_type=jnp.float32).astype(
        jnp.bfloat16
    )
    previous = passed_along(projected[rows_here - (TAPS - 1) :], "seq", 1)
    padded = jnp.concatenate([previous, projected], axis=0).astype(jnp.float32)
    flat_taps = short_taps.reshape(TAPS, 3 * width_here)
    filtered = jnp.zeros((rows_here, 3 * width_here), jnp.float32)
    for shift_back in range(TAPS):
        filtered = (
            filtered
            + flat_taps[shift_back]
            * padded[TAPS - 1 - shift_back : TAPS - 1 - shift_back + rows_here]
        )
    query_stream = filtered[:, :width_here]
    gated_in = filtered[:, width_here : 2 * width_here] * filtered[:, 2 * width_here :]
    block_len = math.gcd(rows_here, 128)
    block_count = rows_here // block_len
    scaled_rates = decay_rates / tokens_all
    offsets_in = jnp.arange(block_len, dtype=jnp.float32)
    distance = jnp.arange(block_len)[:, None] - jnp.arange(block_len)[None, :]
    lag = jnp.maximum(distance, 0).astype(jnp.float32)
    toeplitz = jnp.where(
        (distance >= 0)[None],
        jnp.sum(residues[:, :, None, None] * jnp.exp(-scaled_rates[:, :, None, None] * lag), axis=0),
        0.0,
    )
    blocks_in = gated_in.reshape(block_count, block_len, filter_count, group_width)
    local_part = jnp.einsum("gts,bsgi->btgi", toeplitz, blocks_in, precision=lax.Precision.HIGHEST)
    end_weights = jnp.exp(-scaled_rates[:, :, None] * (block_len - 1 - offsets_in)[None, None, :])
    block_ends = jnp.einsum(
        "mgs,bsgi->bmgi", end_weights, blocks_in, precision=lax.Precision.HIGHEST
    )
    inner_decay = jnp.exp(-scaled_rates * block_len)[:, :, None]
    running = jnp.zeros((mode_count, filter_count, group_width), jnp.float32)
    starts_list = []
    for block_number in range(block_count):
        starts_list.append(running)
        running = inner_decay * running + block_ends[block_number]
    local_starts = jnp.stack(starts_list, axis=0)
    end_state = running.reshape(mode_count, width_here)
    incoming = jnp.zeros((mode_count, width_here), jnp.float32)
    for hops in range(1, lax.axis_size("seq")):
        decayed = jnp.repeat(jnp.exp(-scaled_rates * (rows_here * (hops - 1))), group_width, axis=1)
        incoming = incoming + decayed * passed_along(end_state, "seq", hops)
    block_offsets = (jnp.arange(block_count, dtype=jnp.float32) * block_len)[:, None, None]
    start_decay = jnp.exp(-scaled_rates[None] * block_offsets)
    block_starts = (
        local_starts
        + start_decay[..., None] * incoming.reshape(mode_count, filter_count, group_width)[None]
    )
    carry_weights = residues[None] * jnp.exp(
        -scaled_rates[None] * (offsets_in + 1.0)[:, None, None]
    )
    carried = jnp.einsum(
        "tmg,bmgi->btgi", carry_weights, block_starts, precision=lax.Precision.HIGHEST
    )
    convolved = (local_part + carried).reshape(rows_here, width_here)
    gated_out = (query_stream * convolved).astype(jnp.bfloat16)
    turned = sum_over_channels(project_out(out_weight_pair, gated_out))
    mixed = turned.T.astype(jnp.bfloat16)
    return mixed


def fine_mesh(mesh):
    devices = mesh.devices
    coords = [d.coords for d in devices.flat]
    nx = len({c[0] for c in coords})
    nz = len({c[2] for c in coords})
    return Mesh(devices.reshape(devices.shape[0], nx, nz, devices.shape[1] // (nx * nz)), ("seq",) + CH)


def solution(mesh):
    in_specs = (
        P("seq", CH),
        P(None, None, CH),
        P(None, None, CH),
        P(None, CH),
        P(None, CH),
        P(CH, None),
    )
    out_specs = P("seq", CH)
    return jax.shard_map(
        on_device, mesh=fine_mesh(mesh), in_specs=in_specs, out_specs=out_specs, check_vma=False
    )
```

```python
import math

import jax
import jax.numpy as jnp
from jax import lax
from jax.sharding import Mesh, PartitionSpec as P

TAPS = 3


def passed_along(block, axis, distance):
    devices = range(lax.axis_size(axis))
    route = [(i - distance, i) for i in devices if i - distance in devices]
    return lax.ppermute(block, axis, route)


CH = ("x", "z", "core")


def spread_to(block, axis):
    count = lax.axis_size(axis)
    return lax.all_to_all(jnp.broadcast_to(block[None], (count,) + block.shape), axis, 0, 0, tiled=True)


def gather_features(tokens):
    rows = tokens.shape[0]
    every = spread_to(spread_to(spread_to(tokens, "z"), "x"), "core")
    return every.transpose(3, 1, 2, 0, 4).reshape(rows, -1)


def summed_over(parts, axis):
    got = lax.all_to_all(parts.astype(jnp.bfloat16), axis, 0, 0, tiled=True)
    return jnp.sum(got.astype(jnp.float32), axis=0)


def pair_rows(out_weight):
    rows, model_width = out_weight.shape
    nx, nz = lax.axis_size("x"), lax.axis_size("z")
    width = model_width // (nx * nz * 2)
    split = out_weight.reshape(rows, nx, nz, 2, width).transpose(3, 0, 1, 2, 4)
    return lax.all_to_all(split, "core", 0, 0, tiled=True)


def project_out(weight_pair, gated_out):
    both = jnp.broadcast_to(gated_out[None], (2,) + gated_out.shape)
    inputs_pair = lax.all_to_all(both, "core", 0, 0, tiled=True)
    return jnp.einsum(
        "crxzw,ctr->xzwt", weight_pair, inputs_pair, preferred_element_type=jnp.float32
    )


def sum_over_channels(partial):
    by_x = summed_over(partial, "x")
    return summed_over(by_x, "z")


def on_device(tokens, in_weight, short_taps, decay_rates, residues, out_weight):
    rows_here = tokens.shape[0]
    width_here = in_weight.shape[2]
    model_width = in_weight.shape[0]
    filter_count = decay_rates.shape[1]
    mode_count = decay_rates.shape[0]
    group_width = width_here // filter_count
    tokens_all = rows_here * lax.axis_size("seq")
    flat_weight = in_weight.reshape(model_width, 3 * width_here)
    out_weight_pair = pair_rows(out_weight)
    gathered = gather_features(tokens)
    projected = jnp.dot(gathered, flat_weight, preferred_element_type=jnp.float32).astype(
        jnp.bfloat16
    )
    previous = passed_along(projected[rows_here - (TAPS - 1) :], "seq", 1)
    padded = jnp.concatenate([previous, projected], axis=0).astype(jnp.float32)
    flat_taps = short_taps.reshape(TAPS, 3 * width_here)
    filtered = jnp.zeros((rows_here, 3 * width_here), jnp.float32)
    for shift_back in range(TAPS):
        filtered = (
            filtered
            + flat_taps[shift_back]
            * padded[TAPS - 1 - shift_back : TAPS - 1 - shift_back + rows_here]
        )
    query_stream = filtered[:, :width_here]
    gated_in = filtered[:, width_here : 2 * width_here] * filtered[:, 2 * width_here :]
    block_len = math.gcd(rows_here, 128)
    block_count = rows_here // block_len
    scaled_rates = decay_rates / tokens_all
    offsets_in = jnp.arange(block_len, dtype=jnp.float32)
    distance = jnp.arange(block_len)[:, None] - jnp.arange(block_len)[None, :]
    lag = jnp.maximum(distance, 0).astype(jnp.float32)
    toeplitz = jnp.where(
        (distance >= 0)[None],
        jnp.sum(residues[:, :, None, None] * jnp.exp(-scaled_rates[:, :, None, None] * lag), axis=0),
        0.0,
    )
    blocks_in = gated_in.reshape(block_count, block_len, filter_count, group_width)
    local_part = jnp.einsum("gts,bsgi->btgi", toeplitz, blocks_in, precision=lax.Precision.HIGHEST)
    end_weights = jnp.exp(-scaled_rates[:, :, None] * (block_len - 1 - offsets_in)[None, None, :])
    block_ends = jnp.einsum(
        "mgs,bsgi->bmgi", end_weights, blocks_in, precision=lax.Precision.HIGHEST
    )
    inner_decay = jnp.exp(-scaled_rates * block_len)[:, :, None]
    running = jnp.zeros((mode_count, filter_count, group_width), jnp.float32)
    starts_list = []
    for block_number in range(block_count):
        starts_list.append(running)
        running = inner_decay * running + block_ends[block_number]
    local_starts = jnp.stack(starts_list, axis=0)
    end_state = running.reshape(mode_count, width_here)
    incoming = jnp.zeros((mode_count, width_here), jnp.float32)
    for hops in range(1, lax.axis_size("seq")):
        decayed = jnp.repeat(jnp.exp(-scaled_rates * (rows_here * (hops - 1))), group_width, axis=1)
        incoming = incoming + decayed * passed_along(end_state, "seq", hops)
    block_offsets = (jnp.arange(block_count, dtype=jnp.float32) * block_len)[:, None, None]
    start_decay = jnp.exp(-scaled_rates[None] * block_offsets)
    block_starts = (
        local_starts
        + start_decay[..., None] * incoming.reshape(mode_count, filter_count, group_width)[None]
    )
    carry_weights = residues[None] * jnp.exp(
        -scaled_rates[None] * (offsets_in + 1.0)[:, None, None]
    )
    carried = jnp.einsum(
        "tmg,bmgi->btgi", carry_weights, block_starts, precision=lax.Precision.HIGHEST
    )
    convolved = (local_part + carried).reshape(rows_here, width_here)
    gated_out = (query_stream * convolved).astype(jnp.bfloat16)
    turned = sum_over_channels(project_out(out_weight_pair, gated_out))
    mixed = turned.T.astype(jnp.bfloat16)
    return mixed


def fine_mesh(mesh):
    devices = mesh.devices
    coords = [d.coords for d in devices.flat]
    nx = len({c[0] for c in coords})
    nz = len({c[2] for c in coords})
    return Mesh(devices.reshape(devices.shape[0], nx, nz, devices.shape[1] // (nx * nz)), ("seq",) + CH)


def solution(mesh):
    in_specs = (
        P("seq", CH),
        P(None, None, CH),
        P(None, None, CH),
        P(None, CH),
        P(None, CH),
        P(CH, None),
    )
    out_specs = P("seq", CH)
    return jax.shard_map(
        on_device, mesh=fine_mesh(mesh), in_specs=in_specs, out_specs=out_specs, check_vma=False
    )
```

```python
import math

import jax
import jax.numpy as jnp
from jax import lax
from jax.sharding import Mesh, PartitionSpec as P

TAPS = 3


def passed_along(block, axis, distance):
    devices = range(lax.axis_size(axis))
    route = [(i - distance, i) for i in devices if i - distance in devices]
    return lax.ppermute(block, axis, route)


CH = ("x", "z", "core")


def spread_to(block, axis):
    count = lax.axis_size(axis)
    return lax.all_to_all(jnp.broadcast_to(block[None], (count,) + block.shape), axis, 0, 0, tiled=True)


def gather_features(tokens):
    rows = tokens.shape[0]
    every = spread_to(spread_to(spread_to(tokens, "z"), "x"), "core")
    return every.transpose(3, 1, 2, 0, 4).reshape(rows, -1)


def summed_over(parts, axis):
    got = lax.all_to_all(parts.astype(jnp.bfloat16), axis, 0, 0, tiled=True)
    return jnp.sum(got.astype(jnp.float32), axis=0)


def pair_rows(out_weight):
    rows, model_width = out_weight.shape
    nx, nz = lax.axis_size("x"), lax.axis_size("z")
    width = model_width // (nx * nz * 2)
    split = out_weight.reshape(rows, nx, nz, 2, width).transpose(3, 0, 1, 2, 4)
    return lax.all_to_all(split, "core", 0, 0, tiled=True)


def project_out(weight_pair, gated_out):
    both = jnp.broadcast_to(gated_out[None], (2,) + gated_out.shape)
    inputs_pair = lax.all_to_all(both, "core", 0, 0, tiled=True)
    return jnp.einsum(
        "crxzw,ctr->xzwt", weight_pair, inputs_pair, preferred_element_type=jnp.float32
    )


def sum_over_channels(partial):
    by_x = summed_over(partial, "x")
    return summed_over(by_x, "z")


def from_earlier_blocks(end_state, block_rates, group_width):
    blocks = lax.axis_size("seq")
    here = lax.axis_index("seq")
    ends = spread_to(end_state, "seq")
    source = jnp.arange(blocks)
    between = jnp.maximum(here - 1 - source, 0).astype(jnp.float32)
    decay = jnp.where(
        (source < here)[:, None, None],
        jnp.exp(-block_rates[None] * between[:, None, None]),
        0.0,
    )
    return jnp.sum(jnp.repeat(decay, group_width, axis=2) * ends, axis=0)


def on_device(tokens, in_weight, short_taps, decay_rates, residues, out_weight):
    rows_here = tokens.shape[0]
    width_here = in_weight.shape[2]
    model_width = in_weight.shape[0]
    filter_count = decay_rates.shape[1]
    mode_count = decay_rates.shape[0]
    group_width = width_here // filter_count
    tokens_all = rows_here * lax.axis_size("seq")
    flat_weight = in_weight.reshape(model_width, 3 * width_here)
    out_weight_pair = pair_rows(out_weight)
    gathered = gather_features(tokens)
    projected = jnp.dot(gathered, flat_weight, preferred_element_type=jnp.float32).astype(
        jnp.bfloat16
    )
    previous = passed_along(projected[rows_here - (TAPS - 1) :], "seq", 1)
    padded = jnp.concatenate([previous, projected], axis=0).astype(jnp.float32)
    flat_taps = short_taps.reshape(TAPS, 3 * width_here)
    filtered = jnp.zeros((rows_here, 3 * width_here), jnp.float32)
    for shift_back in range(TAPS):
        filtered = (
            filtered
            + flat_taps[shift_back]
            * padded[TAPS - 1 - shift_back : TAPS - 1 - shift_back + rows_here]
        )
    query_stream = filtered[:, :width_here]
    gated_in = filtered[:, width_here : 2 * width_here] * filtered[:, 2 * width_here :]
    block_len = math.gcd(rows_here, 128)
    block_count = rows_here // block_len
    scaled_rates = decay_rates / tokens_all
    offsets_in = jnp.arange(block_len, dtype=jnp.float32)
    distance = jnp.arange(block_len)[:, None] - jnp.arange(block_len)[None, :]
    lag = jnp.maximum(distance, 0).astype(jnp.float32)
    toeplitz = jnp.where(
        (distance >= 0)[None],
        jnp.sum(residues[:, :, None, None] * jnp.exp(-scaled_rates[:, :, None, None] * lag), axis=0),
        0.0,
    )
    blocks_in = gated_in.reshape(block_count, block_len, filter_count, group_width)
    local_part = jnp.einsum("gts,bsgi->btgi", toeplitz, blocks_in, precision=lax.Precision.HIGHEST)
    end_weights = jnp.exp(-scaled_rates[:, :, None] * (block_len - 1 - offsets_in)[None, None, :])
    block_ends = jnp.einsum(
        "mgs,bsgi->bmgi", end_weights, blocks_in, precision=lax.Precision.HIGHEST
    )
    inner_decay = jnp.exp(-scaled_rates * block_len)[:, :, None]
    running = jnp.zeros((mode_count, filter_count, group_width), jnp.float32)
    starts_list = []
    for block_number in range(block_count):
        starts_list.append(running)
        running = inner_decay * running + block_ends[block_number]
    local_starts = jnp.stack(starts_list, axis=0)
    end_state = running.reshape(mode_count, width_here)
    incoming = from_earlier_blocks(end_state, scaled_rates * rows_here, group_width)
    block_offsets = (jnp.arange(block_count, dtype=jnp.float32) * block_len)[:, None, None]
    start_decay = jnp.exp(-scaled_rates[None] * block_offsets)
    block_starts = (
        local_starts
        + start_decay[..., None] * incoming.reshape(mode_count, filter_count, group_width)[None]
    )
    carry_weights = residues[None] * jnp.exp(
        -scaled_rates[None] * (offsets_in + 1.0)[:, None, None]
    )
    carried = jnp.einsum(
        "tmg,bmgi->btgi", carry_weights, block_starts, precision=lax.Precision.HIGHEST
    )
    convolved = (local_part + carried).reshape(rows_here, width_here)
    gated_out = (query_stream * convolved).astype(jnp.bfloat16)
    turned = sum_over_channels(project_out(out_weight_pair, gated_out))
    mixed = turned.T.astype(jnp.bfloat16)
    return mixed


def fine_mesh(mesh):
    devices = mesh.devices
    coords = [d.coords for d in devices.flat]
    nx = len({c[0] for c in coords})
    nz = len({c[2] for c in coords})
    return Mesh(devices.reshape(devices.shape[0], nx, nz, devices.shape[1] // (nx * nz)), ("seq",) + CH)


def solution(mesh):
    in_specs = (
        P("seq", CH),
        P(None, None, CH),
        P(None, None, CH),
        P(None, CH),
        P(None, CH),
        P(CH, None),
    )
    out_specs = P("seq", CH)
    return jax.shard_map(
        on_device, mesh=fine_mesh(mesh), in_specs=in_specs, out_specs=out_specs, check_vma=False
    )
```

```python
import math

import jax
import jax.numpy as jnp
from jax import lax
from jax.sharding import Mesh, PartitionSpec as P

TAPS = 3


def passed_along(block, axis, distance):
    devices = range(lax.axis_size(axis))
    route = [(i - distance, i) for i in devices if i - distance in devices]
    return lax.ppermute(block, axis, route)


CH = ("x", "z", "core")


def spread_to(block, axis):
    count = lax.axis_size(axis)
    return lax.all_to_all(jnp.broadcast_to(block[None], (count,) + block.shape), axis, 0, 0, tiled=True)


def gather_features(tokens):
    rows = tokens.shape[0]
    along_z = spread_to(tokens, "z")
    every = spread_to(spread_to(along_z, "x"), "core")
    return every.transpose(3, 1, 2, 0, 4).reshape(rows, -1)


def summed_over(parts, axis):
    got = lax.all_to_all(parts.astype(jnp.bfloat16), axis, 0, 0, tiled=True)
    return jnp.sum(got.astype(jnp.float32), axis=0)


def pair_rows(out_weight):
    rows, model_width = out_weight.shape
    nx, nz = lax.axis_size("x"), lax.axis_size("z")
    width = model_width // (nx * nz * 2)
    split = out_weight.reshape(rows, nx, nz, 2, width).transpose(1, 3, 0, 2, 4)
    return lax.all_to_all(split.reshape(nx * 2, rows, nz, width), ("x", "core"), 0, 0, tiled=True)


def project_out(weight_pair, gated_out):
    inputs_pair = spread_to(gated_out, ("x", "core"))
    return jnp.einsum(
        "krzw,ktr->zwt", weight_pair, inputs_pair, preferred_element_type=jnp.float32
    )


def sum_over_channels(partial):
    return summed_over(partial, "z")


def from_earlier_blocks(end_state, block_rates, group_width):
    blocks = lax.axis_size("seq")
    here = lax.axis_index("seq")
    ends = spread_to(end_state, "seq")
    source = jnp.arange(blocks)
    between = jnp.maximum(here - 1 - source, 0).astype(jnp.float32)
    decay = jnp.where(
        (source < here)[:, None, None],
        jnp.exp(-block_rates[None] * between[:, None, None]),
        0.0,
    )
    return jnp.sum(jnp.repeat(decay, group_width, axis=2) * ends, axis=0)


def on_device(tokens, in_weight, short_taps, decay_rates, residues, out_weight):
    rows_here = tokens.shape[0]
    width_here = in_weight.shape[2]
    model_width = in_weight.shape[0]
    filter_count = decay_rates.shape[1]
    mode_count = decay_rates.shape[0]
    group_width = width_here // filter_count
    tokens_all = rows_here * lax.axis_size("seq")
    flat_weight = in_weight.reshape(model_width, 3 * width_here)
    out_weight_pair = pair_rows(out_weight)
    gathered = gather_features(tokens)
    projected = jnp.dot(gathered, flat_weight, preferred_element_type=jnp.float32).astype(
        jnp.bfloat16
    )
    previous = passed_along(projected[rows_here - (TAPS - 1) :], "seq", 1)
    padded = jnp.concatenate([previous, projected], axis=0).astype(jnp.float32)
    flat_taps = short_taps.reshape(TAPS, 3 * width_here)
    filtered = jnp.zeros((rows_here, 3 * width_here), jnp.float32)
    for shift_back in range(TAPS):
        filtered = (
            filtered
            + flat_taps[shift_back]
            * padded[TAPS - 1 - shift_back : TAPS - 1 - shift_back + rows_here]
        )
    query_stream = filtered[:, :width_here]
    gated_in = filtered[:, width_here : 2 * width_here] * filtered[:, 2 * width_here :]
    block_len = math.gcd(rows_here, 128)
    block_count = rows_here // block_len
    scaled_rates = decay_rates / tokens_all
    offsets_in = jnp.arange(block_len, dtype=jnp.float32)
    distance = jnp.arange(block_len)[:, None] - jnp.arange(block_len)[None, :]
    lag = jnp.maximum(distance, 0).astype(jnp.float32)
    toeplitz = jnp.where(
        (distance >= 0)[None],
        jnp.sum(residues[:, :, None, None] * jnp.exp(-scaled_rates[:, :, None, None] * lag), axis=0),
        0.0,
    )
    blocks_in = gated_in.reshape(block_count, block_len, filter_count, group_width)
    local_part = jnp.einsum("gts,bsgi->btgi", toeplitz, blocks_in, precision=lax.Precision.HIGHEST)
    end_weights = jnp.exp(-scaled_rates[:, :, None] * (block_len - 1 - offsets_in)[None, None, :])
    block_ends = jnp.einsum(
        "mgs,bsgi->bmgi", end_weights, blocks_in, precision=lax.Precision.HIGHEST
    )
    inner_decay = jnp.exp(-scaled_rates * block_len)[:, :, None]
    running = jnp.zeros((mode_count, filter_count, group_width), jnp.float32)
    starts_list = []
    for block_number in range(block_count):
        starts_list.append(running)
        running = inner_decay * running + block_ends[block_number]
    local_starts = jnp.stack(starts_list, axis=0)
    end_state = running.reshape(mode_count, width_here)
    incoming = from_earlier_blocks(end_state, scaled_rates * rows_here, group_width)
    block_offsets = (jnp.arange(block_count, dtype=jnp.float32) * block_len)[:, None, None]
    start_decay = jnp.exp(-scaled_rates[None] * block_offsets)
    block_starts = (
        local_starts
        + start_decay[..., None] * incoming.reshape(mode_count, filter_count, group_width)[None]
    )
    carry_weights = residues[None] * jnp.exp(
        -scaled_rates[None] * (offsets_in + 1.0)[:, None, None]
    )
    carried = jnp.einsum(
        "tmg,bmgi->btgi", carry_weights, block_starts, precision=lax.Precision.HIGHEST
    )
    convolved = (local_part + carried).reshape(rows_here, width_here)
    gated_out = (query_stream * convolved).astype(jnp.bfloat16)
    turned = sum_over_channels(project_out(out_weight_pair, gated_out))
    mixed = turned.T.astype(jnp.bfloat16)
    return mixed


def fine_mesh(mesh):
    devices = mesh.devices
    coords = [d.coords for d in devices.flat]
    nx = len({c[0] for c in coords})
    nz = len({c[2] for c in coords})
    return Mesh(devices.reshape(devices.shape[0], nx, nz, devices.shape[1] // (nx * nz)), ("seq",) + CH)


def solution(mesh):
    in_specs = (
        P("seq", CH),
        P(None, None, CH),
        P(None, None, CH),
        P(None, CH),
        P(None, CH),
        P(CH, None),
    )
    out_specs = P("seq", CH)
    return jax.shard_map(on_device, mesh=fine_mesh(mesh), in_specs=in_specs, out_specs=out_specs, check_vma=False)
```

```python
import math

import jax
import jax.numpy as jnp
from jax import lax
from jax.sharding import Mesh, PartitionSpec as P

TAPS = 3


def passed_along(block, axis, distance):
    devices = range(lax.axis_size(axis))
    route = [(i - distance, i) for i in devices if i - distance in devices]
    return lax.ppermute(block, axis, route)


CH = ("x", "z", "core")


def spread_to(block, axis):
    count = lax.axis_size(axis)
    return lax.all_to_all(jnp.broadcast_to(block[None], (count,) + block.shape), axis, 0, 0, tiled=True)


def gather_features(tokens):
    rows = tokens.shape[0]
    every = spread_to(spread_to(spread_to(tokens, "z"), "x"), "core")
    return every.transpose(3, 1, 2, 0, 4).reshape(rows, -1)


def summed_over(parts, axis):
    got = lax.all_to_all(parts.astype(jnp.bfloat16), axis, 0, 0, tiled=True)
    return jnp.sum(got.astype(jnp.float32), axis=0)


def project_out(out_weight, gated_out):
    rows, model_width = out_weight.shape
    nx, nz = lax.axis_size("x"), lax.axis_size("z")
    width = model_width // (nx * nz * 2)
    split = out_weight.reshape(rows, nx, nz, 2, width).transpose(3, 0, 1, 2, 4)
    both = jnp.broadcast_to(gated_out[None], (2,) + gated_out.shape)
    sent = jnp.concatenate([split.reshape(2, -1), both.reshape(2, -1)], axis=1)
    got = lax.all_to_all(sent, "core", 0, 0, tiled=True)
    weight_pair = got[:, : split[0].size].reshape(split.shape)
    inputs_pair = got[:, split[0].size :].reshape(both.shape)
    return jnp.einsum(
        "crxzw,ctr->xzwt", weight_pair, inputs_pair, preferred_element_type=jnp.float32
    )


def sum_over_channels(partial):
    by_x = summed_over(partial, "x")
    return summed_over(by_x, "z")


def from_earlier_blocks(end_state, block_rates, group_width):
    blocks = lax.axis_size("seq")
    here = lax.axis_index("seq")
    ends = spread_to(end_state, "seq")
    source = jnp.arange(blocks)
    between = jnp.maximum(here - 1 - source, 0).astype(jnp.float32)
    decay = jnp.where(
        (source < here)[:, None, None],
        jnp.exp(-block_rates[None] * between[:, None, None]),
        0.0,
    )
    return jnp.sum(jnp.repeat(decay, group_width, axis=2) * ends, axis=0)


def on_device(tokens, in_weight, short_taps, decay_rates, residues, out_weight):
    rows_here = tokens.shape[0]
    width_here = in_weight.shape[2]
    model_width = in_weight.shape[0]
    filter_count = decay_rates.shape[1]
    mode_count = decay_rates.shape[0]
    group_width = width_here // filter_count
    tokens_all = rows_here * lax.axis_size("seq")
    flat_weight = in_weight.reshape(model_width, 3 * width_here)
    gathered = gather_features(tokens)
    projected = jnp.dot(gathered, flat_weight, preferred_element_type=jnp.float32).astype(
        jnp.bfloat16
    )
    previous = passed_along(projected[rows_here - (TAPS - 1) :], "seq", 1)
    padded = jnp.concatenate([previous, projected], axis=0).astype(jnp.float32)
    flat_taps = short_taps.reshape(TAPS, 3 * width_here)
    filtered = jnp.zeros((rows_here, 3 * width_here), jnp.float32)
    for shift_back in range(TAPS):
        filtered = (
            filtered
            + flat_taps[shift_back]
            * padded[TAPS - 1 - shift_back : TAPS - 1 - shift_back + rows_here]
        )
    query_stream = filtered[:, :width_here]
    gated_in = filtered[:, width_here : 2 * width_here] * filtered[:, 2 * width_here :]
    block_len = math.gcd(rows_here, 128)
    block_count = rows_here // block_len
    scaled_rates = decay_rates / tokens_all
    offsets_in = jnp.arange(block_len, dtype=jnp.float32)
    distance = jnp.arange(block_len)[:, None] - jnp.arange(block_len)[None, :]
    lag = jnp.maximum(distance, 0).astype(jnp.float32)
    toeplitz = jnp.where(
        (distance >= 0)[None],
        jnp.sum(residues[:, :, None, None] * jnp.exp(-scaled_rates[:, :, None, None] * lag), axis=0),
        0.0,
    )
    blocks_in = gated_in.reshape(block_count, block_len, filter_count, group_width)
    local_part = jnp.einsum("gts,bsgi->btgi", toeplitz, blocks_in, precision=lax.Precision.HIGHEST)
    end_weights = jnp.exp(-scaled_rates[:, :, None] * (block_len - 1 - offsets_in)[None, None, :])
    block_ends = jnp.einsum(
        "mgs,bsgi->bmgi", end_weights, blocks_in, precision=lax.Precision.HIGHEST
    )
    inner_decay = jnp.exp(-scaled_rates * block_len)[:, :, None]
    running = jnp.zeros((mode_count, filter_count, group_width), jnp.float32)
    starts_list = []
    for block_number in range(block_count):
        starts_list.append(running)
        running = inner_decay * running + block_ends[block_number]
    local_starts = jnp.stack(starts_list, axis=0)
    end_state = running.reshape(mode_count, width_here)
    incoming = from_earlier_blocks(end_state, scaled_rates * rows_here, group_width)
    block_offsets = (jnp.arange(block_count, dtype=jnp.float32) * block_len)[:, None, None]
    start_decay = jnp.exp(-scaled_rates[None] * block_offsets)
    block_starts = (
        local_starts
        + start_decay[..., None] * incoming.reshape(mode_count, filter_count, group_width)[None]
    )
    carry_weights = residues[None] * jnp.exp(
        -scaled_rates[None] * (offsets_in + 1.0)[:, None, None]
    )
    carried = jnp.einsum(
        "tmg,bmgi->btgi", carry_weights, block_starts, precision=lax.Precision.HIGHEST
    )
    convolved = (local_part + carried).reshape(rows_here, width_here)
    gated_out = (query_stream * convolved).astype(jnp.bfloat16)
    turned = sum_over_channels(project_out(out_weight, gated_out))
    mixed = turned.T.astype(jnp.bfloat16)
    return mixed


def fine_mesh(mesh):
    devices = mesh.devices
    coords = [d.coords for d in devices.flat]
    nx = len({c[0] for c in coords})
    nz = len({c[2] for c in coords})
    return Mesh(devices.reshape(devices.shape[0], nx, nz, devices.shape[1] // (nx * nz)), ("seq",) + CH)


def solution(mesh):
    in_specs = (
        P("seq", CH),
        P(None, None, CH),
        P(None, None, CH),
        P(None, CH),
        P(None, CH),
        P(CH, None),
    )
    out_specs = P("seq", CH)
    return jax.shard_map(
        on_device, mesh=fine_mesh(mesh), in_specs=in_specs, out_specs=out_specs, check_vma=False
    )
```

```python
import math

import jax
import jax.numpy as jnp
from jax import lax
from jax.sharding import Mesh, PartitionSpec as P

TAPS = 3


def passed_along(block, axis, distance):
    devices = range(lax.axis_size(axis))
    route = [(i - distance, i) for i in devices if i - distance in devices]
    return lax.ppermute(block, axis, route)


CH = ("x", "z", "core")


def spread_to(block, axis):
    count = lax.axis_size(axis)
    return lax.all_to_all(jnp.broadcast_to(block[None], (count,) + block.shape), axis, 0, 0, tiled=True)


def gather_features(tokens):
    rows = tokens.shape[0]
    every = spread_to(spread_to(spread_to(tokens, "z"), "x"), "core")
    return every.transpose(3, 1, 2, 0, 4).reshape(rows, -1)


def summed_over(parts, axis):
    got = lax.all_to_all(parts.astype(jnp.bfloat16), axis, 0, 0, tiled=True)
    return jnp.sum(got.astype(jnp.float32), axis=0)


def pair_rows(out_weight):
    rows, model_width = out_weight.shape
    nx, nz = lax.axis_size("x"), lax.axis_size("z")
    width = model_width // (nx * nz * 2)
    split = out_weight.reshape(rows, nx, nz, 2, width).transpose(3, 0, 1, 2, 4)
    return lax.all_to_all(split, "core", 0, 0, tiled=True)


def project_out(weight_pair, gated_out):
    both = jnp.broadcast_to(gated_out[None], (2,) + gated_out.shape)
    inputs_pair = lax.all_to_all(both, "core", 0, 0, tiled=True)
    return jnp.einsum(
        "crxzw,ctr->xzwt", weight_pair, inputs_pair, preferred_element_type=jnp.float32
    )


def sum_over_channels(partial):
    by_x = summed_over(partial, "x")
    return summed_over(by_x, "z")


def from_earlier_blocks(end_state, block_rates, group_width):
    blocks = lax.axis_size("seq")
    here = lax.axis_index("seq")
    ends = spread_to(end_state, "seq")
    source = jnp.arange(blocks)
    between = jnp.maximum(here - 1 - source, 0).astype(jnp.float32)
    decay = jnp.where(
        (source < here)[:, None, None],
        jnp.exp(-block_rates[None] * between[:, None, None]),
        0.0,
    )
    return jnp.sum(jnp.repeat(decay, group_width, axis=2) * ends, axis=0)


def on_device(tokens, in_weight, short_taps, decay_rates, residues, out_weight):
    rows_here = tokens.shape[0]
    width_here = in_weight.shape[2]
    model_width = in_weight.shape[0]
    filter_count = decay_rates.shape[1]
    mode_count = decay_rates.shape[0]
    group_width = width_here // filter_count
    tokens_all = rows_here * lax.axis_size("seq")
    flat_weight = in_weight.reshape(model_width, 3 * width_here)
    out_weight_pair = pair_rows(out_weight)
    gathered = gather_features(tokens)
    projected = jnp.dot(gathered, flat_weight, preferred_element_type=jnp.float32).astype(
        jnp.bfloat16
    )
    flat_taps = short_taps.reshape(TAPS, 3 * width_here)
    head = projected[: TAPS - 1].astype(jnp.float32)
    tail = projected[rows_here - (TAPS - 1) :].astype(jnp.float32)

    def gated_with(previous):
        padded = jnp.concatenate([previous, projected.astype(jnp.float32)], axis=0)
        filtered = jnp.zeros((rows_here, 3 * width_here), jnp.float32)
        for shift_back in range(TAPS):
            filtered = (
                filtered
                + flat_taps[shift_back]
                * padded[TAPS - 1 - shift_back : TAPS - 1 - shift_back + rows_here]
            )
        return filtered[:, :width_here], filtered[:, width_here : 2 * width_here] * filtered[:, 2 * width_here :]

    def head_gated(previous, first):
        padded = jnp.concatenate([previous, first], axis=0)
        filtered = jnp.zeros((TAPS - 1, 3 * width_here), jnp.float32)
        for shift_back in range(TAPS):
            filtered = filtered + flat_taps[shift_back] * padded[TAPS - 1 - shift_back : 2 * (TAPS - 1) - shift_back]
        return filtered[:, width_here : 2 * width_here] * filtered[:, 2 * width_here :]

    no_previous = jnp.zeros((TAPS - 1, 3 * width_here), jnp.float32)
    _, gated_alone = gated_with(no_previous)
    block_len = math.gcd(rows_here, 128)
    block_count = rows_here // block_len
    scaled_rates = decay_rates / tokens_all
    offsets_in = jnp.arange(block_len, dtype=jnp.float32)
    end_weights = jnp.exp(-scaled_rates[:, :, None] * (block_len - 1 - offsets_in)[None, None, :])
    inner_decay = jnp.exp(-scaled_rates * block_len)[:, :, None]

    def ends_of(gated):
        blocks = gated.reshape(block_count, block_len, filter_count, group_width)
        ends = jnp.einsum("mgs,bsgi->bmgi", end_weights, blocks, precision=lax.Precision.HIGHEST)
        running = jnp.zeros((mode_count, filter_count, group_width), jnp.float32)
        starts_list = []
        for block_number in range(block_count):
            starts_list.append(running)
            running = inner_decay * running + ends[block_number]
        return jnp.stack(starts_list, axis=0), running.reshape(mode_count, width_here)

    _, end_alone = ends_of(gated_alone)
    packed = jnp.concatenate(
        [end_alone, head.reshape(-1, width_here), tail.reshape(-1, width_here)], axis=0
    )
    every = spread_to(packed, "seq")
    blocks_seq = lax.axis_size("seq")
    here = lax.axis_index("seq")
    source = jnp.arange(blocks_seq)
    heads = every[:, mode_count : mode_count + 3 * (TAPS - 1)].reshape(blocks_seq, TAPS - 1, 3 * width_here)
    tails = every[:, mode_count + 3 * (TAPS - 1) :].reshape(blocks_seq, TAPS - 1, 3 * width_here)
    tails_before = jnp.where(
        (source >= 1)[:, None, None], jnp.roll(tails, 1, axis=0), 0.0
    )
    head_decay = jnp.repeat(
        jnp.exp(-scaled_rates[None] * (rows_here - 1 - jnp.arange(TAPS - 1, dtype=jnp.float32))[:, None, None]),
        group_width,
        axis=2,
    )
    fixes = []
    for j in range(blocks_seq):
        delta = head_gated(tails_before[j], heads[j]) - head_gated(no_previous, heads[j])
        fixes.append(jnp.sum(head_decay * delta[:, None, :], axis=0))
    end_states = every[:, :mode_count] + jnp.stack(fixes, axis=0)
    between = jnp.maximum(here - 1 - source, 0).astype(jnp.float32)
    decay = jnp.where(
        (source < here)[:, None, None],
        jnp.exp(-(scaled_rates * rows_here)[None] * between[:, None, None]),
        0.0,
    )
    incoming = jnp.sum(jnp.repeat(decay, group_width, axis=2) * end_states, axis=0)
    previous = jnp.sum(jnp.where((source == here - 1)[:, None, None], tails, 0.0), axis=0)
    query_stream, gated_in = gated_with(previous)
    distance = jnp.arange(block_len)[:, None] - jnp.arange(block_len)[None, :]
    lag = jnp.maximum(distance, 0).astype(jnp.float32)
    toeplitz = jnp.where(
        (distance >= 0)[None],
        jnp.sum(residues[:, :, None, None] * jnp.exp(-scaled_rates[:, :, None, None] * lag), axis=0),
        0.0,
    )
    blocks_in = gated_in.reshape(block_count, block_len, filter_count, group_width)
    local_part = jnp.einsum("gts,bsgi->btgi", toeplitz, blocks_in, precision=lax.Precision.HIGHEST)
    local_starts, _ = ends_of(gated_in)
    block_offsets = (jnp.arange(block_count, dtype=jnp.float32) * block_len)[:, None, None]
    start_decay = jnp.exp(-scaled_rates[None] * block_offsets)
    block_starts = (
        local_starts
        + start_decay[..., None] * incoming.reshape(mode_count, filter_count, group_width)[None]
    )
    carry_weights = residues[None] * jnp.exp(
        -scaled_rates[None] * (offsets_in + 1.0)[:, None, None]
    )
    carried = jnp.einsum(
        "tmg,bmgi->btgi", carry_weights, block_starts, precision=lax.Precision.HIGHEST
    )
    convolved = (local_part + carried).reshape(rows_here, width_here)
    gated_out = (query_stream * convolved).astype(jnp.bfloat16)
    turned = sum_over_channels(project_out(out_weight_pair, gated_out))
    mixed = turned.T.astype(jnp.bfloat16)
    return mixed


def fine_mesh(mesh):
    devices = mesh.devices
    coords = [d.coords for d in devices.flat]
    nx = len({c[0] for c in coords})
    nz = len({c[2] for c in coords})
    return Mesh(devices.reshape(devices.shape[0], nx, nz, devices.shape[1] // (nx * nz)), ("seq",) + CH)


def solution(mesh):
    in_specs = (
        P("seq", CH),
        P(None, None, CH),
        P(None, None, CH),
        P(None, CH),
        P(None, CH),
        P(CH, None),
    )
    out_specs = P("seq", CH)
    return jax.shard_map(
        on_device, mesh=fine_mesh(mesh), in_specs=in_specs, out_specs=out_specs, check_vma=False
    )
```

```python
import math

import jax
import jax.numpy as jnp
from jax import lax
from jax.sharding import Mesh, PartitionSpec as P

TAPS = 3


def passed_along(block, axis, distance):
    devices = range(lax.axis_size(axis))
    route = [(i - distance, i) for i in devices if i - distance in devices]
    return lax.ppermute(block, axis, route)


CH = ("x", "z", "core")


def spread_to(block, axis):
    count = lax.axis_size(axis)
    return lax.all_to_all(jnp.broadcast_to(block[None], (count,) + block.shape), axis, 0, 0, tiled=True)


def gather_features(tokens):
    rows = tokens.shape[0]
    every = spread_to(spread_to(spread_to(tokens, "z"), "x"), "core")
    return every.transpose(3, 1, 2, 0, 4).reshape(rows, -1)


def summed_over(parts, axis, wire=jnp.bfloat16):
    got = lax.all_to_all(parts.astype(wire), axis, 0, 0, tiled=True)
    return jnp.sum(got.astype(jnp.float32), axis=0)


def pair_rows(out_weight):
    rows, model_width = out_weight.shape
    nx, nz = lax.axis_size("x"), lax.axis_size("z")
    width = model_width // (nx * nz * 2)
    split = out_weight.reshape(rows, nx, nz, 2, width).transpose(3, 0, 1, 2, 4)
    return lax.all_to_all(split, "core", 0, 0, tiled=True)


def project_out(weight_pair, gated_out):
    both = jnp.broadcast_to(gated_out[None], (2,) + gated_out.shape)
    inputs_pair = lax.all_to_all(both, "core", 0, 0, tiled=True)
    return jnp.einsum(
        "crxzw,ctr->xzwt", weight_pair, inputs_pair, preferred_element_type=jnp.float32
    )


def sum_over_channels(partial):
    by_x = summed_over(partial, "x")
    return summed_over(by_x, "z", jnp.float32)


def from_earlier_blocks(end_state, block_rates, group_width):
    blocks = lax.axis_size("seq")
    here = lax.axis_index("seq")
    ends = spread_to(end_state, "seq")
    source = jnp.arange(blocks)
    between = jnp.maximum(here - 1 - source, 0).astype(jnp.float32)
    decay = jnp.where(
        (source < here)[:, None, None],
        jnp.exp(-block_rates[None] * between[:, None, None]),
        0.0,
    )
    return jnp.sum(jnp.repeat(decay, group_width, axis=2) * ends, axis=0)


def on_device(tokens, in_weight, short_taps, decay_rates, residues, out_weight):
    rows_here = tokens.shape[0]
    width_here = in_weight.shape[2]
    model_width = in_weight.shape[0]
    filter_count = decay_rates.shape[1]
    mode_count = decay_rates.shape[0]
    group_width = width_here // filter_count
    tokens_all = rows_here * lax.axis_size("seq")
    flat_weight = in_weight.reshape(model_width, 3 * width_here)
    out_weight_pair = pair_rows(out_weight)
    gathered = gather_features(tokens)
    projected = jnp.dot(gathered, flat_weight, preferred_element_type=jnp.float32).astype(
        jnp.bfloat16
    )
    flat_taps = short_taps.reshape(TAPS, 3 * width_here)
    head = projected[: TAPS - 1].astype(jnp.float32)
    tail = projected[rows_here - (TAPS - 1) :].astype(jnp.float32)

    def gated_with(previous):
        padded = jnp.concatenate([previous, projected.astype(jnp.float32)], axis=0)
        filtered = jnp.zeros((rows_here, 3 * width_here), jnp.float32)
        for shift_back in range(TAPS):
            filtered = (
                filtered
                + flat_taps[shift_back]
                * padded[TAPS - 1 - shift_back : TAPS - 1 - shift_back + rows_here]
            )
        return filtered[:, :width_here], filtered[:, width_here : 2 * width_here] * filtered[:, 2 * width_here :]

    def head_gated(previous, first):
        padded = jnp.concatenate([previous, first], axis=0)
        filtered = jnp.zeros((TAPS - 1, 3 * width_here), jnp.float32)
        for shift_back in range(TAPS):
            filtered = filtered + flat_taps[shift_back] * padded[TAPS - 1 - shift_back : 2 * (TAPS - 1) - shift_back]
        return filtered[:, width_here : 2 * width_here] * filtered[:, 2 * width_here :]

    no_previous = jnp.zeros((TAPS - 1, 3 * width_here), jnp.float32)
    _, gated_alone = gated_with(no_previous)
    block_len = math.gcd(rows_here, 128)
    block_count = rows_here // block_len
    scaled_rates = decay_rates / tokens_all
    offsets_in = jnp.arange(block_len, dtype=jnp.float32)
    end_weights = jnp.exp(-scaled_rates[:, :, None] * (block_len - 1 - offsets_in)[None, None, :])
    inner_decay = jnp.exp(-scaled_rates * block_len)[:, :, None]

    def ends_of(gated):
        blocks = gated.reshape(block_count, block_len, filter_count, group_width)
        ends = jnp.einsum("mgs,bsgi->bmgi", end_weights, blocks, precision=lax.Precision.HIGHEST)
        running = jnp.zeros((mode_count, filter_count, group_width), jnp.float32)
        starts_list = []
        for block_number in range(block_count):
            starts_list.append(running)
            running = inner_decay * running + ends[block_number]
        return jnp.stack(starts_list, axis=0), running.reshape(mode_count, width_here)

    _, end_alone = ends_of(gated_alone)
    packed = jnp.concatenate(
        [end_alone, head.reshape(-1, width_here), tail.reshape(-1, width_here)], axis=0
    )
    every = spread_to(packed, "seq")
    blocks_seq = lax.axis_size("seq")
    here = lax.axis_index("seq")
    source = jnp.arange(blocks_seq)
    heads = every[:, mode_count : mode_count + 3 * (TAPS - 1)].reshape(blocks_seq, TAPS - 1, 3 * width_here)
    tails = every[:, mode_count + 3 * (TAPS - 1) :].reshape(blocks_seq, TAPS - 1, 3 * width_here)
    tails_before = jnp.where(
        (source >= 1)[:, None, None], jnp.roll(tails, 1, axis=0), 0.0
    )
    head_decay = jnp.repeat(
        jnp.exp(-scaled_rates[None] * (rows_here - 1 - jnp.arange(TAPS - 1, dtype=jnp.float32))[:, None, None]),
        group_width,
        axis=2,
    )
    fixes = []
    for j in range(blocks_seq):
        delta = head_gated(tails_before[j], heads[j]) - head_gated(no_previous, heads[j])
        fixes.append(jnp.sum(head_decay * delta[:, None, :], axis=0))
    end_states = every[:, :mode_count] + jnp.stack(fixes, axis=0)
    between = jnp.maximum(here - 1 - source, 0).astype(jnp.float32)
    decay = jnp.where(
        (source < here)[:, None, None],
        jnp.exp(-(scaled_rates * rows_here)[None] * between[:, None, None]),
        0.0,
    )
    incoming = jnp.sum(jnp.repeat(decay, group_width, axis=2) * end_states, axis=0)
    previous = jnp.sum(jnp.where((source == here - 1)[:, None, None], tails, 0.0), axis=0)
    query_stream, gated_in = gated_with(previous)
    distance = jnp.arange(block_len)[:, None] - jnp.arange(block_len)[None, :]
    lag = jnp.maximum(distance, 0).astype(jnp.float32)
    toeplitz = jnp.where(
        (distance >= 0)[None],
        jnp.sum(residues[:, :, None, None] * jnp.exp(-scaled_rates[:, :, None, None] * lag), axis=0),
        0.0,
    )
    blocks_in = gated_in.reshape(block_count, block_len, filter_count, group_width)
    local_part = jnp.einsum("gts,bsgi->btgi", toeplitz, blocks_in, precision=lax.Precision.HIGHEST)
    local_starts, _ = ends_of(gated_in)
    block_offsets = (jnp.arange(block_count, dtype=jnp.float32) * block_len)[:, None, None]
    start_decay = jnp.exp(-scaled_rates[None] * block_offsets)
    block_starts = (
        local_starts
        + start_decay[..., None] * incoming.reshape(mode_count, filter_count, group_width)[None]
    )
    carry_weights = residues[None] * jnp.exp(
        -scaled_rates[None] * (offsets_in + 1.0)[:, None, None]
    )
    carried = jnp.einsum(
        "tmg,bmgi->btgi", carry_weights, block_starts, precision=lax.Precision.HIGHEST
    )
    convolved = (local_part + carried).reshape(rows_here, width_here)
    gated_out = (query_stream * convolved).astype(jnp.bfloat16)
    turned = sum_over_channels(project_out(out_weight_pair, gated_out))
    mixed = turned.T.astype(jnp.bfloat16)
    return mixed


def fine_mesh(mesh):
    devices = mesh.devices
    coords = [d.coords for d in devices.flat]
    nx = len({c[0] for c in coords})
    nz = len({c[2] for c in coords})
    return Mesh(devices.reshape(devices.shape[0], nx, nz, devices.shape[1] // (nx * nz)), ("seq",) + CH)


def solution(mesh):
    in_specs = (
        P("seq", CH),
        P(None, None, CH),
        P(None, None, CH),
        P(None, CH),
        P(None, CH),
        P(CH, None),
    )
    out_specs = P("seq", CH)
    return jax.shard_map(
        on_device, mesh=fine_mesh(mesh), in_specs=in_specs, out_specs=out_specs, check_vma=False
    )
```
